1024 devices in a mesh: grp: 2 (over y_lo), gx: 16 (over z), yz: 32 (over x, y_hi, core).
Axes of the slice: x: 4, y: 8 (y_hi: 4, y_lo: 2; y = y_hi * 2 + y_lo), z: 16, core: 2. Of those that a mesh axis runs over, the one named last changes fastest.
Arguments:
- rhs: float32 [48, 128, 8, 512], P('gx', 'yz', 'grp'), may hold values from -5 to 5
- coeff: float32 [48, 128, 8], P('gx', 'yz', 'grp'), may hold values from 0.5 to 2
- flags: int32 [48, 128, 8], P('gx', 'yz', 'grp'), may hold values 0 or 1
- basis: float32 [8, 8], replicated, may hold values from -1 to 1, as said below
- eigenvalues: float32 [8], replicated, may hold values from 0.2 to 4
Outputs:
- solution: float32 [48, 128, 8, 512], P('gx', 'yz', 'grp')
The draws below stay inside these ranges and needn't reach their ends.
Inputs may be any that keep to these rules, and one draw needn't show every extreme that they name: basis is orthogonal: its transpose is its inverse.
All inputs are finite; a program needn't handle non-finite values. No bound on the sum of `flags` on one device may be relied on, other than what follows from the above.
Results may differ from the reference program's by a relative error of at most 0.0003.
Values sent between devices are 32-bit elements; how exact they have to be, the bound alone decides.
No kernel may reach another device: no remote copies, remote signals or barrier semaphores. Data moves between devices by JAX's collectives and lax.ppermute only.
A program may use at most 64 MiB of HBM per device.

```python
import math
import jax
import jax.numpy as jnp
import numpy as np
from jax import lax

DEG1 = 8
NODES = 512
ITERS = 2
CHEB = 4
EX = 48
EY = 128
EZ = 8


def draw_rhs(key, part):
    values = jax.random.truncated_normal(key, -5.0, 5.0, (EX, EY, EZ, NODES), jnp.float32)
    return values


def draw_basis(key, part):
    matrix = jax.random.normal(key, (DEG1, DEG1), jnp.float32)
    orthogonal, upper_part = jnp.linalg.qr(matrix)
    return orthogonal


def place_ends(entries, key, least, largest):
    place = [jax.random.randint(jax.random.fold_in(key, axis), (), 0, length) for axis, length in enumerate(entries.shape)]
    main_axis = entries.shape.index(max(entries.shape))
    neighbour = place[:main_axis] + [(place[main_axis] + 1) % entries.shape[main_axis]] + place[main_axis + 1:]
    return entries.at[tuple(place)].set(least).at[tuple(neighbour)].set(largest)


def shard_levels(stream_key, shape, shards, smallest, largest):
    gain = 1.0
    for axis_at, parts in shards:
        steps = jax.random.uniform(jax.random.fold_in(jax.random.fold_in(stream_key, 6), axis_at), (parts,), jnp.float32, smallest / len(shards), largest / len(shards))
        gain = gain * jnp.repeat(jnp.exp(steps), shape[axis_at] // parts).reshape((-1,) + (1,) * (len(shape) - 1 - axis_at))
    return gain


def setup_inputs(seed: int = 0) -> dict:
    seeds = jax.random.split(jax.random.key(seed), 6)
    rhs = draw_rhs(jax.random.fold_in(seeds[5], 71), 0)
    coeff = jnp.clip(jnp.exp(math.log(2.0) - 1.3862944 * jax.random.uniform(seeds[1], (EX, EY, EZ), jnp.float32) ** shard_levels(seeds[1], (EX, EY, EZ), ((0, 16), (1, 32), (2, 2)), -0.2, 0.2)), 0.5, 2.0)
    flags = place_ends((jax.random.randint(seeds[2], (EX, EY, EZ), 0, 2) < 1).astype(jnp.int32), jax.random.fold_in(seeds[2], 1), 0, 1)
    basis = draw_basis(jax.random.fold_in(seeds[5], 71), 0)
    eigenvalues = jnp.clip(jnp.exp(jax.random.uniform(seeds[4], (DEG1,), jnp.float32, math.log(0.2), math.log(4.0))), 0.2, 4.0)
    return {"rhs": rhs, "coeff": coeff, "flags": flags, "basis": basis, "eigenvalues": eigenvalues}


PENALTY = 2.0
COARSE_PENALTY = 1.0
DAMPING = 0.5
CHEB_LOW = 0.1
CHEB_HIGH = 2.0
GLL_POINTS = (-1.0, -0.8717401485096066, -0.5917001814331423, -0.2092992179024789, 0.2092992179024789, 0.5917001814331423, 0.8717401485096066, 1.0)
HIGHEST = lax.Precision.HIGHEST

def build_tables(basis, eigenvalues):
    eigen_table = (basis[:, None, None, :, None, None] * basis[None, :, None, None, :, None] * basis[None, None, :, None, None, :]).reshape(DEG1 ** 3, DEG1 ** 3)
    spectrum = (eigenvalues[:, None, None] + eigenvalues[None, :, None] + eigenvalues[None, None, :]).reshape(-1)
    points = jnp.array(np.array(GLL_POINTS), jnp.float32)
    linear = jnp.stack([(1.0 - points) * 0.5, (1.0 + points) * 0.5])
    restrict_table = (linear.T[:, None, None, :, None, None] * linear.T[None, :, None, None, :, None] * linear.T[None, None, :, None, None, :]).reshape(DEG1 ** 3, 8)
    return (eigen_table, spectrum, restrict_table)

def eigen_apply(values, eigen_table, scale):
    flat = values.reshape(-1, eigen_table.shape[0])
    inside = jnp.dot(flat.astype(jnp.float32), eigen_table.astype(jnp.float32), precision=HIGHEST, preferred_element_type=jnp.float32)
    scaled = inside * scale.reshape(flat.shape)
    back = lax.dot_general(scaled.astype(jnp.float32), eigen_table.astype(jnp.float32), (((1,), (1,)), ((), ())), precision=HIGHEST, preferred_element_type=jnp.float32)
    return back.reshape(values.shape)

def boundary_coefs(flag_values, starts, totals, penalty):
    result_list = []
    for dimension in range(3):
        position = starts[dimension] + lax.broadcasted_iota(jnp.int32, flag_values.shape, dimension)
        lower_coef = penalty * jnp.where(position > 0, 1.0, flag_values)
        upper_coef = penalty * jnp.where(position < totals[dimension] - 1, 1.0, flag_values)
        result_list.append((lower_coef[..., None, None, None], upper_coef[..., None, None, None]))
    return result_list

def neighbour_traces(padded, points):
    lower_list, upper_list = ([], [])
    for dimension in range(3):
        interior = [slice(1, -1)] * 3
        before_index = list(interior)
        before_index[dimension] = slice(0, -2)
        after_index = list(interior)
        after_index[dimension] = slice(2, None)
        lower_list.append(lax.slice_in_dim(padded[tuple(before_index)], points - 1, points, axis=3 + dimension))
        upper_list.append(lax.slice_in_dim(padded[tuple(after_index)], 0, 1, axis=3 + dimension))
    return (lower_list, upper_list)

def face_term(field, lower_list, upper_list, coefs, penalty):
    summed = jnp.zeros_like(field)
    points = field.shape[3]
    for dimension in range(3):
        node_axis = 3 + dimension
        low_face = lax.slice_in_dim(field, 0, 1, axis=node_axis)
        high_face = lax.slice_in_dim(field, points - 1, points, axis=node_axis)
        lower_coef, upper_coef = coefs[dimension]
        low_term = lower_coef * low_face - penalty * lower_list[dimension]
        high_term = upper_coef * high_face - penalty * upper_list[dimension]
        low_pad = [(0, 0)] * 6
        low_pad[node_axis] = (0, points - 1)
        high_pad = [(0, 0)] * 6
        high_pad[node_axis] = (points - 1, 0)
        summed = summed + jnp.pad(low_term, low_pad) + jnp.pad(high_term, high_pad)
    return summed

def coarse_block(corners, coarse_coeff):
    weight = coarse_coeff[..., None, None, None]
    return weight * (3.5 * corners - jnp.flip(corners, 3) - jnp.flip(corners, 4) - jnp.flip(corners, 5))

def chebyshev(coarse_rhs, coarse_coeff, apply_coarse):
    center = 0.5 * (CHEB_HIGH + CHEB_LOW)
    half_width = 0.5 * (CHEB_HIGH - CHEB_LOW)
    sigma_value = center / half_width
    rho_now = 1.0 / sigma_value
    inverse_diag = (1.0 / (coarse_coeff * 3.5 + 3.0 * COARSE_PENALTY))[..., None]
    remain = coarse_rhs
    update = inverse_diag * remain / center
    result = update
    for sweep_num in range(CHEB - 1):
        remain = remain - apply_coarse(update)
        rho_next = 1.0 / (2.0 * sigma_value - rho_now)
        update = rho_next * rho_now * update + 2.0 * rho_next / half_width * (inverse_diag * remain)
        result = result + update
        rho_now = rho_next
    return result

def reference(rhs, coeff, flags, basis, eigenvalues):
    eigen_table, spectrum, restrict_table = build_tables(basis, eigenvalues)
    shape_three = rhs.shape[:3]
    node_count = rhs.shape[3]
    flag_values = flags.astype(jnp.float32)
    fine_coefs = boundary_coefs(flag_values, (0, 0, 0), shape_three, PENALTY)
    coarse_coefs = boundary_coefs(flag_values, (0, 0, 0), shape_three, COARSE_PENALTY)
    block_scale = coeff[..., None] * spectrum
    inverse_scale = 1.0 / block_scale

    def apply_fine(solution):
        field = solution.reshape(shape_three + (DEG1, DEG1, DEG1))
        padded = jnp.pad(field, ((1, 1), (1, 1), (1, 1), (0, 0), (0, 0), (0, 0)))
        lower_list, upper_list = neighbour_traces(padded, DEG1)
        faces = face_term(field, lower_list, upper_list, fine_coefs, PENALTY).reshape(solution.shape)
        return eigen_apply(solution, eigen_table, block_scale) + faces

    def apply_coarse(values):
        corners = values.reshape(values.shape[:3] + (2, 2, 2))
        padded = jnp.pad(corners, ((1, 1), (1, 1), (1, 1), (0, 0), (0, 0), (0, 0)))
        lower_list, upper_list = neighbour_traces(padded, 2)
        faces = face_term(corners, lower_list, upper_list, coarse_coefs, COARSE_PENALTY)
        return (coarse_block(corners, coeff) + faces).reshape(values.shape)
    solution = jnp.zeros_like(rhs)
    for iteration in range(ITERS):
        residual = rhs if iteration == 0 else rhs - apply_fine(solution)
        smoothed = eigen_apply(residual, eigen_table, inverse_scale)
        coarse_rhs = jnp.dot(residual.reshape(-1, node_count).astype(jnp.float32), restrict_table.astype(jnp.float32), precision=HIGHEST, preferred_element_type=jnp.float32).reshape(shape_three + (8,))
        coarse_sol = chebyshev(coarse_rhs, coeff, apply_coarse)
        lifted = lax.dot_general(coarse_sol.reshape(-1, 8).astype(jnp.float32), restrict_table.astype(jnp.float32), (((1,), (1,)), ((), ())), precision=HIGHEST, preferred_element_type=jnp.float32).reshape(rhs.shape)
        solution = solution + DAMPING * (smoothed + lifted)
    return solution
```

```python
import math

import jax
import jax.numpy as jnp
import numpy as np
from jax import lax
from jax.sharding import PartitionSpec as P

DEG1 = 8
ITERS = 2
CHEB = 4


PENALTY = 2.0
COARSE_PENALTY = 1.0
DAMPING = 0.5
CHEB_LOW = 0.1
CHEB_HIGH = 2.0
GLL_POINTS = (
    -1.0,
    -0.8717401485096066,
    -0.5917001814331423,
    -0.2092992179024789,
    0.2092992179024789,
    0.5917001814331423,
    0.8717401485096066,
    1.0,
)
HIGHEST = lax.Precision.HIGHEST
HALO = 2 * (CHEB - 1) + 1


def _constant_tables():
    points = np.array(GLL_POINTS, np.float64)
    linear = np.stack([(1.0 - points) * 0.5, (1.0 + points) * 0.5])
    restrict = np.einsum("ai,bj,ck->ijkabc", linear, linear, linear).reshape(DEG1**3, 8)
    moments = []
    for d in range(3):
        table = np.zeros((DEG1,) * 3 + (2,) * 3)
        for a in np.ndindex(2, 2, 2):
            for n in np.ndindex(DEG1, DEG1, DEG1):
                if n[d] != (DEG1 - 1) * a[d]:
                    continue
                w = 1.0
                for e in range(3):
                    if e != d:
                        w *= linear[a[e], n[e]]
                table[n + a] = w
        moments.append(table.reshape(DEG1**3, 8))
    moments = np.stack(moments)
    transfer = np.einsum("dna,nb->dab", moments, restrict)
    idx = np.arange(DEG1**3)
    picks = [idx // (DEG1 * DEG1), (idx // DEG1) % DEG1, idx % DEG1]
    onehot = np.stack([(p[:, None] == np.arange(DEG1)[None, :]) for p in picks]).astype(np.float32)
    return (
        restrict.astype(np.float32),
        np.concatenate(list(moments), axis=1).astype(np.float32),
        transfer.astype(np.float32),
        onehot,
    )


RESTRICT, MOMENTS, TRANSFER, ONEHOT = _constant_tables()


def mm(a, b):
    return jnp.dot(a, b, precision=HIGHEST, preferred_element_type=jnp.float32)


def mm_t(a, b):
    return lax.dot_general(
        a, b, (((1,), (1,)), ((), ())), precision=HIGHEST, preferred_element_type=jnp.float32
    )


def build_eigen(basis):
    table = None
    for s in ONEHOT:
        s = jnp.asarray(s)
        part = mm_t(mm(s, basis), s)
        table = part if table is None else table * part
    return table


def boundary_coefs(flag_values, starts, totals, penalty):
    result_list = []
    for dimension in range(3):
        position = starts[dimension] + lax.broadcasted_iota(jnp.int32, flag_values.shape, dimension)
        lower_coef = penalty * jnp.where(position > 0, 1.0, flag_values)
        upper_coef = penalty * jnp.where(position < totals[dimension] - 1, 1.0, flag_values)
        result_list.append((lower_coef[..., None, None, None], upper_coef[..., None, None, None]))
    return result_list


def face_term(field, lower_list, upper_list, coefs, penalty):
    summed = jnp.zeros_like(field)
    points = field.shape[3]
    for dimension in range(3):
        node_axis = 3 + dimension
        low_face = lax.slice_in_dim(field, 0, 1, axis=node_axis)
        high_face = lax.slice_in_dim(field, points - 1, points, axis=node_axis)
        lower_coef, upper_coef = coefs[dimension]
        low_term = lower_coef * low_face - penalty * lower_list[dimension]
        high_term = upper_coef * high_face - penalty * upper_list[dimension]
        low_pad = [(0, 0)] * 6
        low_pad[node_axis] = (0, points - 1)
        high_pad = [(0, 0)] * 6
        high_pad[node_axis] = (points - 1, 0)
        summed = summed + jnp.pad(low_term, low_pad) + jnp.pad(high_term, high_pad)
    return summed


def pack(parts):
    return jnp.concatenate([p.reshape(-1) for p in parts])


def unpack(flat, likes):
    out, at = [], 0
    for like in likes:
        size = math.prod(like.shape)
        out.append(flat[at : at + size].reshape(like.shape))
        at += size
    return out


def gather_halo(data, axis, dim, halo, lo_extra, hi_extra):
    n = lax.axis_size(axis)
    block = data.shape[dim]
    width = min(halo, block * (n - 1))
    reach = -(-width // block)
    me = lax.axis_index(axis)
    lows, highs = [], []
    got_lo = got_hi = None
    for k in range(1, reach + 1):
        take = min(block, width - (k - 1) * block)
        lo_piece = lax.slice_in_dim(data, block - take, block, axis=dim)
        hi_piece = lax.slice_in_dim(data, 0, take, axis=dim)
        if k == 1 and n == 2:
            send = jnp.where(me == 0, pack([lo_piece, lo_extra]), pack([hi_piece, hi_extra]))
            got = lax.ppermute(send, axis, [(0, 1), (1, 0)])
            r_piece, r_extra = unpack(got, [lo_piece, lo_extra])
            zero = jnp.zeros_like(r_piece)
            zero_extra = jnp.zeros_like(r_extra)
            lows.append(jnp.where(me == 1, r_piece, zero))
            highs.append(jnp.where(me == 0, r_piece, zero))
            got_lo = jnp.where(me == 1, r_extra, zero_extra)
            got_hi = jnp.where(me == 0, r_extra, zero_extra)
            continue
        up = [(i, i + k) for i in range(n - k)]
        down = [(i + k, i) for i in range(n - k)]
        if k == 1:
            r_lo = lax.ppermute(pack([lo_piece, lo_extra]), axis, up)
            r_hi = lax.ppermute(pack([hi_piece, hi_extra]), axis, down)
            lo_p, got_lo = unpack(r_lo, [lo_piece, lo_extra])
            hi_p, got_hi = unpack(r_hi, [hi_piece, hi_extra])
        else:
            lo_p = lax.ppermute(lo_piece, axis, up)
            hi_p = lax.ppermute(hi_piece, axis, down)
        lows.append(lo_p)
        highs.append(hi_p)
    full = jnp.concatenate(lows[::-1] + [data] + highs, axis=dim)
    return full, width, got_lo, got_hi


def shift(v, axis, s):
    size = v.shape[axis]
    zshape = list(v.shape)
    zshape[axis] = abs(s)
    zeros = jnp.zeros(zshape, v.dtype)
    if s > 0:
        return jnp.concatenate([lax.slice_in_dim(v, s, size, axis=axis), zeros], axis=axis)
    return jnp.concatenate([zeros, lax.slice_in_dim(v, 0, size + s, axis=axis)], axis=axis)


def chebyshev(coarse_rhs, inverse_diag, apply_coarse):
    center = 0.5 * (CHEB_HIGH + CHEB_LOW)
    half_width = 0.5 * (CHEB_HIGH - CHEB_LOW)
    sigma_value = center / half_width
    rho_now = 1.0 / sigma_value
    remain = coarse_rhs
    update = inverse_diag * remain / center
    result = update
    for sweep_num in range(CHEB - 1):
        remain = remain - apply_coarse(update)
        rho_next = 1.0 / (2.0 * sigma_value - rho_now)
        update = rho_next * rho_now * update + 2.0 * rho_next / half_width * (inverse_diag * remain)
        result = result + update
        rho_now = rho_next
    return result


def body(rhs, coeff, flags, basis, eigenvalues):
    bx, by, bz, nodes = rhs.shape
    count = bx * by * bz
    axes = ("gx", "yz", "grp")
    blocks = (bx, by, bz)
    index = [lax.axis_index(a) for a in axes]
    starts = tuple(index[d] * blocks[d] for d in range(3))
    totals = tuple(blocks[d] * lax.axis_size(axes[d]) for d in range(3))
    flag_values = flags.astype(jnp.float32)

    eigen_table = build_eigen(basis)
    spectrum = (
        eigenvalues[:, None, None] + eigenvalues[None, :, None] + eigenvalues[None, None, :]
    ).reshape(-1)
    restrict = jnp.asarray(RESTRICT)
    eig_restrict = lax.dot_general(
        eigen_table, restrict, (((0,), (0,)), ((), ())), precision=HIGHEST,
        preferred_element_type=jnp.float32,
    )
    stiff_restrict = mm(eigen_table, spectrum[:, None] * eig_restrict)
    coarse_stiff = lax.dot_general(
        eig_restrict, spectrum[:, None] * eig_restrict, (((0,), (0,)), ((), ())),
        precision=HIGHEST, preferred_element_type=jnp.float32,
    )

    rhs2 = rhs.reshape(count, nodes)
    coeff2 = coeff.reshape(count, 1)
    block_scale = coeff2 * spectrum[None, :]
    inverse_scale = 1.0 / block_scale
    inside0 = mm(rhs2, eigen_table)
    smooth0 = mm_t(inside0 * inverse_scale, eigen_table)
    q0 = mm(rhs2, restrict)
    mom0 = mm(smooth0, jnp.asarray(MOMENTS))
    packet = jnp.concatenate([q0, mom0, coeff2, flag_values.reshape(count, 1)], axis=1)
    chans = packet.shape[1]
    packet = packet.T.reshape(chans, bx, by, bz)

    s6 = smooth0.reshape(bx, by, bz, DEG1, DEG1, DEG1)
    last = DEG1 - 1
    face_hi = [
        lax.slice_in_dim(lax.slice_in_dim(s6, blocks[d] - 1, blocks[d], axis=d), last, DEG1, axis=3 + d)
        for d in range(3)
    ]
    face_lo = [
        lax.slice_in_dim(lax.slice_in_dim(s6, 0, 1, axis=d), 0, 1, axis=3 + d) for d in range(3)
    ]

    box = packet
    widths = []
    recv_lo, recv_hi = [None] * 3, [None] * 3
    for d in range(3):
        box, w, recv_lo[d], recv_hi[d] = gather_halo(box, axes[d], 1 + d, HALO, face_hi[d], face_lo[d])
        widths.append(w)
    nx, ny, nz = box.shape[1:]
    flat = nx * ny
    box = box.transpose(0, 3, 1, 2).reshape(chans, nz, flat)

    q0b = box[0:8].reshape(2, 2, 2, nz, flat)
    momb = [box[8 + 8 * d : 16 + 8 * d].reshape(2, 2, 2, nz, flat) for d in range(3)]
    coeffb = box[32]
    flagb = box[33]

    pos = []
    for d, n_d in enumerate((nx, ny, nz)):
        pos.append(starts[d] - widths[d] + jnp.arange(n_d, dtype=jnp.int32))
    px = jnp.broadcast_to(pos[0][None, :, None], (nz, nx, ny)).reshape(nz, flat)
    py = jnp.broadcast_to(pos[1][None, None, :], (nz, nx, ny)).reshape(nz, flat)
    pz = jnp.broadcast_to(pos[2][:, None], (nz, flat))
    pvals = (px, py, pz)
    in_domain = (
        (px >= 0) & (px < totals[0]) & (py >= 0) & (py < totals[1]) & (pz >= 0) & (pz < totals[2])
    )
    g_lo = [jnp.where(pvals[d] > 0, 1.0, flagb) for d in range(3)]
    g_hi = [jnp.where(pvals[d] < totals[d] - 1, 1.0, flagb) for d in range(3)]
    moves = ((4, ny), (4, 1), (3, 1))

    def face_dim(v, d, tau):
        ax, st = moves[d]
        low = lax.slice_in_dim(v, 0, 1, axis=d)
        high = lax.slice_in_dim(v, 1, 2, axis=d)
        low_term = tau * g_lo[d] * low - tau * shift(high, ax, -st)
        high_term = tau * g_hi[d] * high - tau * shift(low, ax, st)
        return jnp.concatenate([low_term, high_term], axis=d)

    def apply_coarse(v):
        block = coeffb * (3.5 * v - jnp.flip(v, 0) - jnp.flip(v, 1) - jnp.flip(v, 2))
        faces = face_dim(v, 0, COARSE_PENALTY) + face_dim(v, 1, COARSE_PENALTY) + face_dim(
            v, 2, COARSE_PENALTY
        )
        return block + faces

    def corner_map(table, v):
        v8 = v.reshape(8, nz, flat)
        out = [sum(table[a, b] * v8[b] for b in range(8)) for a in range(8)]
        return jnp.stack(out).reshape(2, 2, 2, nz, flat)

    inverse_diag = jnp.where(in_domain, 1.0 / (coeffb * 3.5 + 3.0 * COARSE_PENALTY), 0.0)
    c0b = chebyshev(q0b, inverse_diag, apply_coarse)
    mom_u1 = [0.5 * (momb[d] + corner_map(TRANSFER[d], c0b)) for d in range(3)]
    rtf = face_dim(mom_u1[0], 0, PENALTY) + face_dim(mom_u1[1], 1, PENALTY) + face_dim(
        mom_u1[2], 2, PENALTY
    )
    gc0 = corner_map(coarse_stiff, c0b)
    q1b = 0.5 * q0b - 0.5 * coeffb * gc0 - rtf
    c1b = chebyshev(q1b, inverse_diag, apply_coarse)

    wx, wy, wz = widths

    def take(cb, xs, ys, zs):
        c4 = cb.reshape(8, nz, nx, ny)[:, zs[0] : zs[1], xs[0] : xs[1], ys[0] : ys[1]]
        c4 = c4.transpose(2, 3, 1, 0)
        return c4.reshape(-1, 8), c4.shape[:3]

    own_x, own_y, own_z = (wx, wx + bx), (wy, wy + by), (wz, wz + bz)
    c0_own, _ = take(c0b, own_x, own_y, own_z)
    c1_own, _ = take(c1b, own_x, own_y, own_z)

    u1 = DAMPING * (smooth0 + mm_t(c0_own, restrict))
    u6 = u1.reshape(bx, by, bz, DEG1, DEG1, DEG1)

    def plane(xs, ys, zs, d, side, recv):
        c, shp = take(c0b, xs, ys, zs)
        lifted = mm_t(c, restrict).reshape(shp + (DEG1,) * 3)
        lifted = lax.slice_in_dim(lifted, side, side + 1, axis=3 + d)
        return DAMPING * (recv + lifted)

    ranges = (own_x, own_y, own_z)
    lower_list, upper_list = [], []
    for d in range(3):
        below = list(ranges)
        below[d] = (ranges[d][0] - 1, ranges[d][0])
        above = list(ranges)
        above[d] = (ranges[d][1], ranges[d][1] + 1)
        p_lo = plane(*below, d, last, recv_lo[d])
        p_hi = plane(*above, d, 0, recv_hi[d])
        inner_hi = lax.slice_in_dim(lax.slice_in_dim(u6, 0, blocks[d] - 1, axis=d), last, DEG1, axis=3 + d)
        inner_lo = lax.slice_in_dim(lax.slice_in_dim(u6, 1, blocks[d], axis=d), 0, 1, axis=3 + d)
        lower_list.append(jnp.concatenate([p_lo, inner_hi], axis=d))
        upper_list.append(jnp.concatenate([inner_lo, p_hi], axis=d))

    fine_coefs = boundary_coefs(flag_values, starts, totals, PENALTY)
    faces = face_term(u6, lower_list, upper_list, fine_coefs, PENALTY).reshape(count, nodes)
    eig_u1 = DAMPING * (rhs2 + coeff2 * mm_t(c0_own, stiff_restrict))
    residual = rhs2 - eig_u1 - faces
    smooth1 = mm_t(mm(residual, eigen_table) * inverse_scale, eigen_table)
    u2 = u1 + DAMPING * (smooth1 + mm_t(c1_own, restrict))
    return u2.reshape(rhs.shape)


def solution(mesh):
    in_specs = (P("gx", "yz", "grp", None), P("gx", "yz", "grp"), P("gx", "yz", "grp"), P(), P())
    out_specs = P("gx", "yz", "grp", None)
    return jax.shard_map(body, mesh=mesh, in_specs=in_specs, out_specs=out_specs, check_vma=False)
```

```python
import jax
import jax.numpy as jnp
import numpy as np
from jax import lax
from jax.sharding import PartitionSpec as P

DEG1 = 8
ITERS = 2
CHEB = 4


PENALTY = 2.0
COARSE_PENALTY = 1.0
DAMPING = 0.5
CHEB_LOW = 0.1
CHEB_HIGH = 2.0
GLL_POINTS = (
    -1.0,
    -0.8717401485096066,
    -0.5917001814331423,
    -0.2092992179024789,
    0.2092992179024789,
    0.5917001814331423,
    0.8717401485096066,
    1.0,
)
HIGHEST = lax.Precision.HIGHEST


def face_traces(field, points):
    lower_list, upper_list = ([], [])
    for dimension, axis in enumerate(("gx", "yz", "grp")):
        count = lax.axis_size(axis)
        block = field.shape[dimension]
        node_axis = 3 + dimension
        high = lax.slice_in_dim(field, points - 1, points, axis=node_axis)
        low = lax.slice_in_dim(field, 0, 1, axis=node_axis)
        top = lax.slice_in_dim(high, block - 1, block, axis=dimension)
        bottom = lax.slice_in_dim(low, 0, 1, axis=dimension)
        if count == 2:
            me = lax.axis_index(axis)
            got = lax.ppermute(jnp.where(me == 0, top, bottom), axis, [(0, 1), (1, 0)])
            zero = jnp.zeros_like(got)
            from_below = jnp.where(me == 1, got, zero)
            from_above = jnp.where(me == 0, got, zero)
        else:
            from_below = lax.ppermute(top, axis, [(i, i + 1) for i in range(count - 1)])
            from_above = lax.ppermute(bottom, axis, [(i + 1, i) for i in range(count - 1)])
        lower_list.append(
            jnp.concatenate([from_below, lax.slice_in_dim(high, 0, block - 1, axis=dimension)], axis=dimension)
        )
        upper_list.append(
            jnp.concatenate([lax.slice_in_dim(low, 1, block, axis=dimension), from_above], axis=dimension)
        )
    return (lower_list, upper_list)


def _onehot_tables():
    idx = np.arange(DEG1**3)
    picks = [idx // (DEG1 * DEG1), (idx // DEG1) % DEG1, idx % DEG1]
    return np.stack([(p[:, None] == np.arange(DEG1)[None, :]) for p in picks]).astype(np.float32)


ONEHOT = _onehot_tables()


def build_tables(basis, eigenvalues):
    eigen_table = None
    for pick in ONEHOT:
        pick = jnp.asarray(pick)
        part = lax.dot_general(
            jnp.dot(pick, basis, precision=HIGHEST, preferred_element_type=jnp.float32),
            pick,
            (((1,), (1,)), ((), ())),
            precision=HIGHEST,
            preferred_element_type=jnp.float32,
        )
        eigen_table = part if eigen_table is None else eigen_table * part
    spectrum = (
        eigenvalues[:, None, None] + eigenvalues[None, :, None] + eigenvalues[None, None, :]
    ).reshape(-1)
    points = jnp.array(np.array(GLL_POINTS), jnp.float32)
    linear = jnp.stack([(1.0 - points) * 0.5, (1.0 + points) * 0.5])
    restrict_table = (
        linear.T[:, None, None, :, None, None]
        * linear.T[None, :, None, None, :, None]
        * linear.T[None, None, :, None, None, :]
    ).reshape(DEG1**3, 8)
    return (eigen_table, spectrum, restrict_table)


def eigen_apply(values, eigen_table, scale):
    flat = values.reshape(-1, eigen_table.shape[0])
    inside = jnp.dot(flat, eigen_table, precision=HIGHEST, preferred_element_type=jnp.float32)
    scaled = inside * scale.reshape(flat.shape)
    back = lax.dot_general(
        scaled,
        eigen_table,
        (((1,), (1,)), ((), ())),
        precision=HIGHEST,
        preferred_element_type=jnp.float32,
    )
    return back.reshape(values.shape)


def boundary_coefs(flag_values, starts, totals, penalty):
    result_list = []
    for dimension in range(3):
        position = starts[dimension] + lax.broadcasted_iota(jnp.int32, flag_values.shape, dimension)
        lower_coef = penalty * jnp.where(position > 0, 1.0, flag_values)
        upper_coef = penalty * jnp.where(position < totals[dimension] - 1, 1.0, flag_values)
        result_list.append((lower_coef[..., None, None, None], upper_coef[..., None, None, None]))
    return result_list


def face_term(field, lower_list, upper_list, coefs, penalty):
    summed = jnp.zeros_like(field)
    points = field.shape[3]
    for dimension in range(3):
        node_axis = 3 + dimension
        low_face = lax.slice_in_dim(field, 0, 1, axis=node_axis)
        high_face = lax.slice_in_dim(field, points - 1, points, axis=node_axis)
        lower_coef, upper_coef = coefs[dimension]
        low_term = lower_coef * low_face - penalty * lower_list[dimension]
        high_term = upper_coef * high_face - penalty * upper_list[dimension]
        low_pad = [(0, 0)] * 6
        low_pad[node_axis] = (0, points - 1)
        high_pad = [(0, 0)] * 6
        high_pad[node_axis] = (points - 1, 0)
        summed = summed + jnp.pad(low_term, low_pad) + jnp.pad(high_term, high_pad)
    return summed


def coarse_block(corners, coarse_coeff):
    weight = coarse_coeff[..., None, None, None]
    return weight * (
        3.5 * corners - jnp.flip(corners, 3) - jnp.flip(corners, 4) - jnp.flip(corners, 5)
    )


def chebyshev(coarse_rhs, coarse_coeff, apply_coarse):
    center = 0.5 * (CHEB_HIGH + CHEB_LOW)
    half_width = 0.5 * (CHEB_HIGH - CHEB_LOW)
    sigma_value = center / half_width
    rho_now = 1.0 / sigma_value
    inverse_diag = (1.0 / (coarse_coeff * 3.5 + 3.0 * COARSE_PENALTY))[..., None]
    remain = coarse_rhs
    update = inverse_diag * remain / center
    result = update
    for sweep_num in range(CHEB - 1):
        remain = remain - apply_coarse(update)
        rho_next = 1.0 / (2.0 * sigma_value - rho_now)
        update = rho_next * rho_now * update + 2.0 * rho_next / half_width * (inverse_diag * remain)
        result = result + update
        rho_now = rho_next
    return result


def body(rhs, coeff, flags, basis, eigenvalues):
    eigen_table, spectrum, restrict_table = build_tables(basis, eigenvalues)
    shape_three = rhs.shape[:3]
    node_count = rhs.shape[3]
    flag_values = flags.astype(jnp.float32)
    starts = (
        lax.axis_index("gx") * shape_three[0],
        lax.axis_index("yz") * shape_three[1],
        lax.axis_index("grp") * shape_three[2],
    )
    totals = (
        shape_three[0] * lax.axis_size("gx"),
        shape_three[1] * lax.axis_size("yz"),
        shape_three[2] * lax.axis_size("grp"),
    )
    fine_coefs = boundary_coefs(flag_values, starts, totals, PENALTY)
    block_scale = coeff[..., None] * spectrum
    inverse_scale = 1.0 / block_scale

    def apply_fine(solution):
        field = solution.reshape(shape_three + (DEG1, DEG1, DEG1))
        lower_list, upper_list = face_traces(field, DEG1)
        faces = face_term(field, lower_list, upper_list, fine_coefs, PENALTY).reshape(
            solution.shape
        )
        return eigen_apply(solution, eigen_table, block_scale) + faces

    solution = jnp.zeros_like(rhs)
    for iteration in range(ITERS):
        residual = rhs if iteration == 0 else rhs - apply_fine(solution)
        smoothed = eigen_apply(residual, eigen_table, inverse_scale)
        coarse_rhs = jnp.dot(
            residual.reshape(-1, node_count),
            restrict_table,
            precision=HIGHEST,
            preferred_element_type=jnp.float32,
        ).reshape(shape_three + (8,))
        own_coefs = boundary_coefs(flag_values, starts, totals, COARSE_PENALTY)

        def apply_own(values):
            corners = values.reshape(values.shape[:3] + (2, 2, 2))
            lower_list, upper_list = face_traces(corners, 2)
            faces = face_term(corners, lower_list, upper_list, own_coefs, COARSE_PENALTY)
            return (coarse_block(corners, coeff) + faces).reshape(values.shape)

        coarse_sol = chebyshev(coarse_rhs, coeff, apply_own)
        lifted = lax.dot_general(
            coarse_sol.reshape(-1, 8),
            restrict_table,
            (((1,), (1,)), ((), ())),
            precision=HIGHEST,
            preferred_element_type=jnp.float32,
        ).reshape(rhs.shape)
        solution = solution + DAMPING * (smoothed + lifted)
    return solution


def solution(mesh):
    in_specs = (P("gx", "yz", "grp", None), P("gx", "yz", "grp"), P("gx", "yz", "grp"), P(), P())
    out_specs = P("gx", "yz", "grp", None)
    return jax.shard_map(body, mesh=mesh, in_specs=in_specs, out_specs=out_specs, check_vma=False)
```

```python
import jax
import jax.numpy as jnp
import numpy as np
from jax import lax
from jax.sharding import PartitionSpec as P

DEG1 = 8
ITERS = 2
CHEB = 4


PENALTY = 2.0
COARSE_PENALTY = 1.0
DAMPING = 0.5
CHEB_LOW = 0.1
CHEB_HIGH = 2.0
GLL_POINTS = (
    -1.0,
    -0.8717401485096066,
    -0.5917001814331423,
    -0.2092992179024789,
    0.2092992179024789,
    0.5917001814331423,
    0.8717401485096066,
    1.0,
)
HIGHEST = lax.Precision.HIGHEST


def face_traces(field, points):
    lower_list, upper_list = ([], [])
    for dimension, axis in enumerate(("gx", "yz", "grp")):
        count = lax.axis_size(axis)
        block = field.shape[dimension]
        node_axis = 3 + dimension
        high = lax.slice_in_dim(field, points - 1, points, axis=node_axis)
        low = lax.slice_in_dim(field, 0, 1, axis=node_axis)
        top = lax.slice_in_dim(high, block - 1, block, axis=dimension)
        bottom = lax.slice_in_dim(low, 0, 1, axis=dimension)
        if count == 2:
            me = lax.axis_index(axis)
            got = lax.ppermute(jnp.where(me == 0, top, bottom), axis, [(0, 1), (1, 0)])
            zero = jnp.zeros_like(got)
            from_below = jnp.where(me == 1, got, zero)
            from_above = jnp.where(me == 0, got, zero)
        else:
            from_below = lax.ppermute(top, axis, [(i, i + 1) for i in range(count - 1)])
            from_above = lax.ppermute(bottom, axis, [(i + 1, i) for i in range(count - 1)])
        lower_list.append(
            jnp.concatenate([from_below, lax.slice_in_dim(high, 0, block - 1, axis=dimension)], axis=dimension)
        )
        upper_list.append(
            jnp.concatenate([lax.slice_in_dim(low, 1, block, axis=dimension), from_above], axis=dimension)
        )
    return (lower_list, upper_list)


def _onehot_tables():
    idx = np.arange(DEG1**3)
    picks = [idx // (DEG1 * DEG1), (idx // DEG1) % DEG1, idx % DEG1]
    return np.stack([(p[:, None] == np.arange(DEG1)[None, :]) for p in picks]).astype(np.float32)


ONEHOT = _onehot_tables()


def face_select():
    n = lax.broadcasted_iota(jnp.int32, (DEG1**3, 6 * 128), 0)
    c = lax.broadcasted_iota(jnp.int32, (DEG1**3, 6 * 128), 1)
    face, spot = c // 128, c % 128
    dim, side = face // 2, face % 2
    n0, n1, n2 = n // (DEG1 * DEG1), (n // DEG1) % DEG1, n % DEG1
    along = jnp.where(dim == 0, n0, jnp.where(dim == 1, n1, n2))
    rest = jnp.where(dim == 0, n1 * DEG1 + n2, jnp.where(dim == 1, n0 * DEG1 + n2, n0 * DEG1 + n1))
    return ((along == side * (DEG1 - 1)) & (spot == rest)).astype(jnp.float32)


def fine_face_term(flat, shape_three, coefs):
    select = face_select()
    faces = jnp.dot(flat, select, precision=HIGHEST, preferred_element_type=jnp.float32)
    faces = faces.reshape(shape_three + (6, 128))
    terms = []
    for dimension, axis in enumerate(("gx", "yz", "grp")):
        count = lax.axis_size(axis)
        block = shape_three[dimension]
        low = faces[..., 2 * dimension, :]
        high = faces[..., 2 * dimension + 1, :]
        top = lax.slice_in_dim(high, block - 1, block, axis=dimension)
        bottom = lax.slice_in_dim(low, 0, 1, axis=dimension)
        if count == 2:
            me = lax.axis_index(axis)
            got = lax.ppermute(jnp.where(me == 0, top, bottom), axis, [(0, 1), (1, 0)])
            zero = jnp.zeros_like(got)
            from_below = jnp.where(me == 1, got, zero)
            from_above = jnp.where(me == 0, got, zero)
        else:
            from_below = lax.ppermute(top, axis, [(i, i + 1) for i in range(count - 1)])
            from_above = lax.ppermute(bottom, axis, [(i + 1, i) for i in range(count - 1)])
        lower = jnp.concatenate([from_below, lax.slice_in_dim(high, 0, block - 1, axis=dimension)], axis=dimension)
        upper = jnp.concatenate([lax.slice_in_dim(low, 1, block, axis=dimension), from_above], axis=dimension)
        lower_coef, upper_coef = coefs[dimension]
        lower_coef = lower_coef.reshape(shape_three + (1,))
        upper_coef = upper_coef.reshape(shape_three + (1,))
        terms.append(lower_coef * low - PENALTY * lower)
        terms.append(upper_coef * high - PENALTY * upper)
    terms = jnp.stack(terms, axis=3).reshape(-1, 6 * 128)
    return lax.dot_general(
        terms, select, (((1,), (1,)), ((), ())), precision=HIGHEST, preferred_element_type=jnp.float32
    )


def build_tables(basis, eigenvalues):
    eigen_table = None
    for pick in ONEHOT:
        pick = jnp.asarray(pick)
        part = lax.dot_general(
            jnp.dot(pick, basis, precision=HIGHEST, preferred_element_type=jnp.float32),
            pick,
            (((1,), (1,)), ((), ())),
            precision=HIGHEST,
            preferred_element_type=jnp.float32,
        )
        eigen_table = part if eigen_table is None else eigen_table * part
    spectrum = (
        eigenvalues[:, None, None] + eigenvalues[None, :, None] + eigenvalues[None, None, :]
    ).reshape(-1)
    points = jnp.array(np.array(GLL_POINTS), jnp.float32)
    linear = jnp.stack([(1.0 - points) * 0.5, (1.0 + points) * 0.5])
    restrict_table = (
        linear.T[:, None, None, :, None, None]
        * linear.T[None, :, None, None, :, None]
        * linear.T[None, None, :, None, None, :]
    ).reshape(DEG1**3, 8)
    return (eigen_table, spectrum, restrict_table)


def eigen_apply(values, eigen_table, scale):
    flat = values.reshape(-1, eigen_table.shape[0])
    inside = jnp.dot(flat, eigen_table, precision=HIGHEST, preferred_element_type=jnp.float32)
    scaled = inside * scale.reshape(flat.shape)
    back = lax.dot_general(
        scaled,
        eigen_table,
        (((1,), (1,)), ((), ())),
        precision=HIGHEST,
        preferred_element_type=jnp.float32,
    )
    return back.reshape(values.shape)


def boundary_coefs(flag_values, starts, totals, penalty):
    result_list = []
    for dimension in range(3):
        position = starts[dimension] + lax.broadcasted_iota(jnp.int32, flag_values.shape, dimension)
        lower_coef = penalty * jnp.where(position > 0, 1.0, flag_values)
        upper_coef = penalty * jnp.where(position < totals[dimension] - 1, 1.0, flag_values)
        result_list.append((lower_coef[..., None, None, None], upper_coef[..., None, None, None]))
    return result_list


def face_term(field, lower_list, upper_list, coefs, penalty):
    summed = jnp.zeros_like(field)
    points = field.shape[3]
    for dimension in range(3):
        node_axis = 3 + dimension
        low_face = lax.slice_in_dim(field, 0, 1, axis=node_axis)
        high_face = lax.slice_in_dim(field, points - 1, points, axis=node_axis)
        lower_coef, upper_coef = coefs[dimension]
        low_term = lower_coef * low_face - penalty * lower_list[dimension]
        high_term = upper_coef * high_face - penalty * upper_list[dimension]
        low_pad = [(0, 0)] * 6
        low_pad[node_axis] = (0, points - 1)
        high_pad = [(0, 0)] * 6
        high_pad[node_axis] = (points - 1, 0)
        summed = summed + jnp.pad(low_term, low_pad) + jnp.pad(high_term, high_pad)
    return summed


def coarse_block(corners, coarse_coeff):
    weight = coarse_coeff[..., None, None, None]
    return weight * (
        3.5 * corners - jnp.flip(corners, 3) - jnp.flip(corners, 4) - jnp.flip(corners, 5)
    )


def chebyshev(coarse_rhs, coarse_coeff, apply_coarse):
    center = 0.5 * (CHEB_HIGH + CHEB_LOW)
    half_width = 0.5 * (CHEB_HIGH - CHEB_LOW)
    sigma_value = center / half_width
    rho_now = 1.0 / sigma_value
    inverse_diag = (1.0 / (coarse_coeff * 3.5 + 3.0 * COARSE_PENALTY))[..., None]
    remain = coarse_rhs
    update = inverse_diag * remain / center
    result = update
    for sweep_num in range(CHEB - 1):
        remain = remain - apply_coarse(update)
        rho_next = 1.0 / (2.0 * sigma_value - rho_now)
        update = rho_next * rho_now * update + 2.0 * rho_next / half_width * (inverse_diag * remain)
        result = result + update
        rho_now = rho_next
    return result


def body(rhs, coeff, flags, basis, eigenvalues):
    eigen_table, spectrum, restrict_table = build_tables(basis, eigenvalues)
    shape_three = rhs.shape[:3]
    node_count = rhs.shape[3]
    flag_values = flags.astype(jnp.float32)
    starts = (
        lax.axis_index("gx") * shape_three[0],
        lax.axis_index("yz") * shape_three[1],
        lax.axis_index("grp") * shape_three[2],
    )
    totals = (
        shape_three[0] * lax.axis_size("gx"),
        shape_three[1] * lax.axis_size("yz"),
        shape_three[2] * lax.axis_size("grp"),
    )
    fine_coefs = boundary_coefs(flag_values, starts, totals, PENALTY)
    block_scale = coeff[..., None] * spectrum
    inverse_scale = 1.0 / block_scale

    def apply_fine(solution):
        faces = fine_face_term(solution.reshape(-1, node_count), shape_three, fine_coefs).reshape(
            solution.shape
        )
        return eigen_apply(solution, eigen_table, block_scale) + faces

    solution = jnp.zeros_like(rhs)
    for iteration in range(ITERS):
        residual = rhs if iteration == 0 else rhs - apply_fine(solution)
        smoothed = eigen_apply(residual, eigen_table, inverse_scale)
        coarse_rhs = jnp.dot(
            residual.reshape(-1, node_count),
            restrict_table,
            precision=HIGHEST,
            preferred_element_type=jnp.float32,
        ).reshape(shape_three + (8,))
        own_coefs = boundary_coefs(flag_values, starts, totals, COARSE_PENALTY)

        def apply_own(values):
            corners = values.reshape(values.shape[:3] + (2, 2, 2))
            lower_list, upper_list = face_traces(corners, 2)
            faces = face_term(corners, lower_list, upper_list, own_coefs, COARSE_PENALTY)
            return (coarse_block(corners, coeff) + faces).reshape(values.shape)

        coarse_sol = chebyshev(coarse_rhs, coeff, apply_own)
        lifted = lax.dot_general(
            coarse_sol.reshape(-1, 8),
            restrict_table,
            (((1,), (1,)), ((), ())),
            precision=HIGHEST,
            preferred_element_type=jnp.float32,
        ).reshape(rhs.shape)
        solution = solution + DAMPING * (smoothed + lifted)
    return solution


def solution(mesh):
    in_specs = (P("gx", "yz", "grp", None), P("gx", "yz", "grp"), P("gx", "yz", "grp"), P(), P())
    out_specs = P("gx", "yz", "grp", None)
    return jax.shard_map(body, mesh=mesh, in_specs=in_specs, out_specs=out_specs, check_vma=False)
```

```python
import jax
import jax.numpy as jnp
import numpy as np
from jax import lax
from jax.sharding import PartitionSpec as P

DEG1 = 8
ITERS = 2
CHEB = 4


PENALTY = 2.0
COARSE_PENALTY = 1.0
DAMPING = 0.5
CHEB_LOW = 0.1
CHEB_HIGH = 2.0
GLL_POINTS = (
    -1.0,
    -0.8717401485096066,
    -0.5917001814331423,
    -0.2092992179024789,
    0.2092992179024789,
    0.5917001814331423,
    0.8717401485096066,
    1.0,
)
HIGHEST = lax.Precision.HIGHEST


def face_traces(field, points):
    lower_list, upper_list = ([], [])
    for dimension, axis in enumerate(("gx", "yz", "grp")):
        count = lax.axis_size(axis)
        block = field.shape[dimension]
        node_axis = 3 + dimension
        high = lax.slice_in_dim(field, points - 1, points, axis=node_axis)
        low = lax.slice_in_dim(field, 0, 1, axis=node_axis)
        top = lax.slice_in_dim(high, block - 1, block, axis=dimension)
        bottom = lax.slice_in_dim(low, 0, 1, axis=dimension)
        if count == 2:
            me = lax.axis_index(axis)
            got = lax.ppermute(jnp.where(me == 0, top, bottom), axis, [(0, 1), (1, 0)])
            zero = jnp.zeros_like(got)
            from_below = jnp.where(me == 1, got, zero)
            from_above = jnp.where(me == 0, got, zero)
        else:
            from_below = lax.ppermute(top, axis, [(i, i + 1) for i in range(count - 1)])
            from_above = lax.ppermute(bottom, axis, [(i + 1, i) for i in range(count - 1)])
        lower_list.append(
            jnp.concatenate([from_below, lax.slice_in_dim(high, 0, block - 1, axis=dimension)], axis=dimension)
        )
        upper_list.append(
            jnp.concatenate([lax.slice_in_dim(low, 1, block, axis=dimension), from_above], axis=dimension)
        )
    return (lower_list, upper_list)


def shift(v, axis, s):
    size = v.shape[axis]
    zshape = list(v.shape)
    zshape[axis] = abs(s)
    zeros = jnp.zeros(zshape, v.dtype)
    if s > 0:
        return jnp.concatenate([lax.slice_in_dim(v, s, size, axis=axis), zeros], axis=axis)
    return jnp.concatenate([zeros, lax.slice_in_dim(v, 0, size + s, axis=axis)], axis=axis)


def halo_box(packet, width):
    for dim, axis in ((1, "gx"), (2, "yz"), (3, "grp")):
        count = lax.axis_size(axis)
        block = packet.shape[dim]
        lo_piece = lax.slice_in_dim(packet, block - width, block, axis=dim)
        hi_piece = lax.slice_in_dim(packet, 0, width, axis=dim)
        if count == 2:
            me = lax.axis_index(axis)
            got = lax.ppermute(jnp.where(me == 0, lo_piece, hi_piece), axis, [(0, 1), (1, 0)])
            zero = jnp.zeros_like(got)
            from_below = jnp.where(me == 1, got, zero)
            from_above = jnp.where(me == 0, got, zero)
        else:
            from_below = lax.ppermute(lo_piece, axis, [(i, i + 1) for i in range(count - 1)])
            from_above = lax.ppermute(hi_piece, axis, [(i + 1, i) for i in range(count - 1)])
        packet = jnp.concatenate([from_below, packet, from_above], axis=dim)
    return packet


def box_solver(coeff, flag_values, starts, totals, width):
    bx, by, bz = coeff.shape
    nx, ny, nz = bx + 2 * width, by + 2 * width, bz + 2 * width
    flat = nx * ny
    state = {}

    def to_box(chans):
        c = chans.shape[0]
        return chans.transpose(0, 3, 1, 2).reshape(c, nz, flat)

    def setup(coeffb, flagb):
        pos = [starts[d] - width + jnp.arange(n, dtype=jnp.int32) for d, n in enumerate((nx, ny, nz))]
        px = jnp.broadcast_to(pos[0][None, :, None], (nz, nx, ny)).reshape(nz, flat)
        py = jnp.broadcast_to(pos[1][None, None, :], (nz, nx, ny)).reshape(nz, flat)
        pz = jnp.broadcast_to(pos[2][:, None], (nz, flat))
        pvals = (px, py, pz)
        in_domain = (
            (px >= 0) & (px < totals[0]) & (py >= 0) & (py < totals[1]) & (pz >= 0) & (pz < totals[2])
        )
        state["coeff"] = coeffb
        state["g_lo"] = [jnp.where(pvals[d] > 0, 1.0, flagb) for d in range(3)]
        state["g_hi"] = [jnp.where(pvals[d] < totals[d] - 1, 1.0, flagb) for d in range(3)]
        state["inverse_diag"] = jnp.where(
            in_domain, 1.0 / (coeffb * 3.5 + 3.0 * COARSE_PENALTY), 0.0
        )

    moves = ((4, ny), (4, 1), (3, 1))

    def face_dim(v, d):
        ax, st = moves[d]
        low = lax.slice_in_dim(v, 0, 1, axis=d)
        high = lax.slice_in_dim(v, 1, 2, axis=d)
        tau = COARSE_PENALTY
        low_term = tau * state["g_lo"][d] * low - tau * shift(high, ax, -st)
        high_term = tau * state["g_hi"][d] * high - tau * shift(low, ax, st)
        return jnp.concatenate([low_term, high_term], axis=d)

    def apply_coarse(v):
        block = state["coeff"] * (3.5 * v - jnp.flip(v, 0) - jnp.flip(v, 1) - jnp.flip(v, 2))
        faces = face_dim(v, 0) + face_dim(v, 1) + face_dim(v, 2)
        return block + faces

    def solve(coarse_rhs):
        chans = coarse_rhs.transpose(3, 0, 1, 2)
        first = not state
        if first:
            chans = jnp.concatenate([chans, jnp.stack([coeff, flag_values])], axis=0)
        box = to_box(halo_box(chans, width))
        if first:
            setup(box[8], box[9])
            box = box[:8]
        box = box.reshape(2, 2, 2, nz, flat)
        inverse_diag = state["inverse_diag"]
        center = 0.5 * (CHEB_HIGH + CHEB_LOW)
        half_width = 0.5 * (CHEB_HIGH - CHEB_LOW)
        sigma_value = center / half_width
        rho_now = 1.0 / sigma_value
        remain = box
        update = inverse_diag * remain / center
        result = update
        for sweep_num in range(CHEB - 1):
            remain = remain - apply_coarse(update)
            rho_next = 1.0 / (2.0 * sigma_value - rho_now)
            update = rho_next * rho_now * update + 2.0 * rho_next / half_width * (inverse_diag * remain)
            result = result + update
            rho_now = rho_next
        own = result.reshape(8, nz, nx, ny)[:, width : width + bz, width : width + bx, width : width + by]
        return own.transpose(2, 3, 1, 0)

    return solve

def _onehot_tables():
    idx = np.arange(DEG1**3)
    picks = [idx // (DEG1 * DEG1), (idx // DEG1) % DEG1, idx % DEG1]
    return np.stack([(p[:, None] == np.arange(DEG1)[None, :]) for p in picks]).astype(np.float32)


ONEHOT = _onehot_tables()


def face_select():
    n = lax.broadcasted_iota(jnp.int32, (DEG1**3, 6 * 128), 0)
    c = lax.broadcasted_iota(jnp.int32, (DEG1**3, 6 * 128), 1)
    face, spot = c // 128, c % 128
    dim, side = face // 2, face % 2
    n0, n1, n2 = n // (DEG1 * DEG1), (n // DEG1) % DEG1, n % DEG1
    along = jnp.where(dim == 0, n0, jnp.where(dim == 1, n1, n2))
    rest = jnp.where(dim == 0, n1 * DEG1 + n2, jnp.where(dim == 1, n0 * DEG1 + n2, n0 * DEG1 + n1))
    return ((along == side * (DEG1 - 1)) & (spot == rest)).astype(jnp.float32)


def fine_face_term(flat, shape_three, coefs):
    select = face_select()
    faces = jnp.dot(flat, select, precision=HIGHEST, preferred_element_type=jnp.float32)
    faces = faces.reshape(shape_three + (6, 128))
    terms = []
    for dimension, axis in enumerate(("gx", "yz", "grp")):
        count = lax.axis_size(axis)
        block = shape_three[dimension]
        low = faces[..., 2 * dimension, :]
        high = faces[..., 2 * dimension + 1, :]
        top = lax.slice_in_dim(high, block - 1, block, axis=dimension)
        bottom = lax.slice_in_dim(low, 0, 1, axis=dimension)
        if count == 2:
            me = lax.axis_index(axis)
            got = lax.ppermute(jnp.where(me == 0, top, bottom), axis, [(0, 1), (1, 0)])
            zero = jnp.zeros_like(got)
            from_below = jnp.where(me == 1, got, zero)
            from_above = jnp.where(me == 0, got, zero)
        else:
            from_below = lax.ppermute(top, axis, [(i, i + 1) for i in range(count - 1)])
            from_above = lax.ppermute(bottom, axis, [(i + 1, i) for i in range(count - 1)])
        lower = jnp.concatenate([from_below, lax.slice_in_dim(high, 0, block - 1, axis=dimension)], axis=dimension)
        upper = jnp.concatenate([lax.slice_in_dim(low, 1, block, axis=dimension), from_above], axis=dimension)
        lower_coef, upper_coef = coefs[dimension]
        lower_coef = lower_coef.reshape(shape_three + (1,))
        upper_coef = upper_coef.reshape(shape_three + (1,))
        terms.append(lower_coef * low - PENALTY * lower)
        terms.append(upper_coef * high - PENALTY * upper)
    terms = jnp.stack(terms, axis=3).reshape(-1, 6 * 128)
    return lax.dot_general(
        terms, select, (((1,), (1,)), ((), ())), precision=HIGHEST, preferred_element_type=jnp.float32
    )


def build_tables(basis, eigenvalues):
    eigen_table = None
    for pick in ONEHOT:
        pick = jnp.asarray(pick)
        part = lax.dot_general(
            jnp.dot(pick, basis, precision=HIGHEST, preferred_element_type=jnp.float32),
            pick,
            (((1,), (1,)), ((), ())),
            precision=HIGHEST,
            preferred_element_type=jnp.float32,
        )
        eigen_table = part if eigen_table is None else eigen_table * part
    spectrum = (
        eigenvalues[:, None, None] + eigenvalues[None, :, None] + eigenvalues[None, None, :]
    ).reshape(-1)
    points = jnp.array(np.array(GLL_POINTS), jnp.float32)
    linear = jnp.stack([(1.0 - points) * 0.5, (1.0 + points) * 0.5])
    restrict_table = (
        linear.T[:, None, None, :, None, None]
        * linear.T[None, :, None, None, :, None]
        * linear.T[None, None, :, None, None, :]
    ).reshape(DEG1**3, 8)
    return (eigen_table, spectrum, restrict_table)


def eigen_apply(values, eigen_table, scale):
    flat = values.reshape(-1, eigen_table.shape[0])
    inside = jnp.dot(flat, eigen_table, precision=HIGHEST, preferred_element_type=jnp.float32)
    scaled = inside * scale.reshape(flat.shape)
    back = lax.dot_general(
        scaled,
        eigen_table,
        (((1,), (1,)), ((), ())),
        precision=HIGHEST,
        preferred_element_type=jnp.float32,
    )
    return back.reshape(values.shape)


def boundary_coefs(flag_values, starts, totals, penalty):
    result_list = []
    for dimension in range(3):
        position = starts[dimension] + lax.broadcasted_iota(jnp.int32, flag_values.shape, dimension)
        lower_coef = penalty * jnp.where(position > 0, 1.0, flag_values)
        upper_coef = penalty * jnp.where(position < totals[dimension] - 1, 1.0, flag_values)
        result_list.append((lower_coef[..., None, None, None], upper_coef[..., None, None, None]))
    return result_list


def face_term(field, lower_list, upper_list, coefs, penalty):
    summed = jnp.zeros_like(field)
    points = field.shape[3]
    for dimension in range(3):
        node_axis = 3 + dimension
        low_face = lax.slice_in_dim(field, 0, 1, axis=node_axis)
        high_face = lax.slice_in_dim(field, points - 1, points, axis=node_axis)
        lower_coef, upper_coef = coefs[dimension]
        low_term = lower_coef * low_face - penalty * lower_list[dimension]
        high_term = upper_coef * high_face - penalty * upper_list[dimension]
        low_pad = [(0, 0)] * 6
        low_pad[node_axis] = (0, points - 1)
        high_pad = [(0, 0)] * 6
        high_pad[node_axis] = (points - 1, 0)
        summed = summed + jnp.pad(low_term, low_pad) + jnp.pad(high_term, high_pad)
    return summed


def coarse_block(corners, coarse_coeff):
    weight = coarse_coeff[..., None, None, None]
    return weight * (
        3.5 * corners - jnp.flip(corners, 3) - jnp.flip(corners, 4) - jnp.flip(corners, 5)
    )


def chebyshev(coarse_rhs, coarse_coeff, apply_coarse):
    center = 0.5 * (CHEB_HIGH + CHEB_LOW)
    half_width = 0.5 * (CHEB_HIGH - CHEB_LOW)
    sigma_value = center / half_width
    rho_now = 1.0 / sigma_value
    inverse_diag = (1.0 / (coarse_coeff * 3.5 + 3.0 * COARSE_PENALTY))[..., None]
    remain = coarse_rhs
    update = inverse_diag * remain / center
    result = update
    for sweep_num in range(CHEB - 1):
        remain = remain - apply_coarse(update)
        rho_next = 1.0 / (2.0 * sigma_value - rho_now)
        update = rho_next * rho_now * update + 2.0 * rho_next / half_width * (inverse_diag * remain)
        result = result + update
        rho_now = rho_next
    return result


def body(rhs, coeff, flags, basis, eigenvalues):
    eigen_table, spectrum, restrict_table = build_tables(basis, eigenvalues)
    shape_three = rhs.shape[:3]
    node_count = rhs.shape[3]
    flag_values = flags.astype(jnp.float32)
    starts = (
        lax.axis_index("gx") * shape_three[0],
        lax.axis_index("yz") * shape_three[1],
        lax.axis_index("grp") * shape_three[2],
    )
    totals = (
        shape_three[0] * lax.axis_size("gx"),
        shape_three[1] * lax.axis_size("yz"),
        shape_three[2] * lax.axis_size("grp"),
    )
    fine_coefs = boundary_coefs(flag_values, starts, totals, PENALTY)
    block_scale = coeff[..., None] * spectrum
    inverse_scale = 1.0 / block_scale

    def apply_fine(solution):
        faces = fine_face_term(solution.reshape(-1, node_count), shape_three, fine_coefs).reshape(
            solution.shape
        )
        return eigen_apply(solution, eigen_table, block_scale) + faces

    solve_coarse = box_solver(coeff, flag_values, starts, totals, CHEB - 1)
    solution = jnp.zeros_like(rhs)
    for iteration in range(ITERS):
        residual = rhs if iteration == 0 else rhs - apply_fine(solution)
        smoothed = eigen_apply(residual, eigen_table, inverse_scale)
        coarse_rhs = jnp.dot(
            residual.reshape(-1, node_count),
            restrict_table,
            precision=HIGHEST,
            preferred_element_type=jnp.float32,
        ).reshape(shape_three + (8,))
        coarse_sol = solve_coarse(coarse_rhs)
        lifted = lax.dot_general(
            coarse_sol.reshape(-1, 8),
            restrict_table,
            (((1,), (1,)), ((), ())),
            precision=HIGHEST,
            preferred_element_type=jnp.float32,
        ).reshape(rhs.shape)
        solution = solution + DAMPING * (smoothed + lifted)
    return solution


def solution(mesh):
    in_specs = (P("gx", "yz", "grp", None), P("gx", "yz", "grp"), P("gx", "yz", "grp"), P(), P())
    out_specs = P("gx", "yz", "grp", None)
    return jax.shard_map(body, mesh=mesh, in_specs=in_specs, out_specs=out_specs, check_vma=False)
```

```python
import jax
import jax.numpy as jnp
import numpy as np
from jax import lax
from jax.sharding import PartitionSpec as P

DEG1 = 8
ITERS = 2
CHEB = 4


PENALTY = 2.0
COARSE_PENALTY = 1.0
DAMPING = 0.5
CHEB_LOW = 0.1
CHEB_HIGH = 2.0
GLL_POINTS = (
    -1.0,
    -0.8717401485096066,
    -0.5917001814331423,
    -0.2092992179024789,
    0.2092992179024789,
    0.5917001814331423,
    0.8717401485096066,
    1.0,
)
HIGHEST = lax.Precision.HIGHEST


def face_traces(field, points):
    lower_list, upper_list = ([], [])
    for dimension, axis in enumerate(("gx", "yz", "grp")):
        count = lax.axis_size(axis)
        block = field.shape[dimension]
        node_axis = 3 + dimension
        high = lax.slice_in_dim(field, points - 1, points, axis=node_axis)
        low = lax.slice_in_dim(field, 0, 1, axis=node_axis)
        top = lax.slice_in_dim(high, block - 1, block, axis=dimension)
        bottom = lax.slice_in_dim(low, 0, 1, axis=dimension)
        if count == 2:
            me = lax.axis_index(axis)
            got = lax.ppermute(jnp.where(me == 0, top, bottom), axis, [(0, 1), (1, 0)])
            zero = jnp.zeros_like(got)
            from_below = jnp.where(me == 1, got, zero)
            from_above = jnp.where(me == 0, got, zero)
        else:
            from_below = lax.ppermute(top, axis, [(i, i + 1) for i in range(count - 1)])
            from_above = lax.ppermute(bottom, axis, [(i + 1, i) for i in range(count - 1)])
        lower_list.append(
            jnp.concatenate([from_below, lax.slice_in_dim(high, 0, block - 1, axis=dimension)], axis=dimension)
        )
        upper_list.append(
            jnp.concatenate([lax.slice_in_dim(low, 1, block, axis=dimension), from_above], axis=dimension)
        )
    return (lower_list, upper_list)


def shift(v, axis, s):
    size = v.shape[axis]
    zshape = list(v.shape)
    zshape[axis] = abs(s)
    zeros = jnp.zeros(zshape, v.dtype)
    if s > 0:
        return jnp.concatenate([lax.slice_in_dim(v, s, size, axis=axis), zeros], axis=axis)
    return jnp.concatenate([zeros, lax.slice_in_dim(v, 0, size + s, axis=axis)], axis=axis)


def pack(parts):
    return jnp.concatenate([p.reshape(-1) for p in parts])


def unpack(flat, likes):
    out, at = [], 0
    for like in likes:
        size = like.size
        out.append(flat[at : at + size].reshape(like.shape))
        at += size
    return out


def halo_box(packet, width, extras=None):
    extras = extras or {}
    received = {}
    for dim, axis in ((3, "grp"), (2, "yz"), (1, "gx")):
        count = lax.axis_size(axis)
        block = packet.shape[dim]
        reach = -(-width // block)
        lows, highs = [], []
        for k in range(1, reach + 1):
            take = min(block, width - (k - 1) * block)
            lo_piece = lax.slice_in_dim(packet, block - take, block, axis=dim)
            hi_piece = lax.slice_in_dim(packet, 0, take, axis=dim)
            lo_send, hi_send = [lo_piece], [hi_piece]
            if k == 1 and axis in extras:
                lo_send.append(extras[axis][0])
                hi_send.append(extras[axis][1])
            if count == 2:
                me = lax.axis_index(axis)
                got = lax.ppermute(jnp.where(me == 0, pack(lo_send), pack(hi_send)), axis, [(0, 1), (1, 0)])
                got = unpack(got, lo_send)
                lo_got = [jnp.where(me == 1, g, jnp.zeros_like(g)) for g in got]
                hi_got = [jnp.where(me == 0, g, jnp.zeros_like(g)) for g in got]
            else:
                up = [(i, i + k) for i in range(count - k)]
                down = [(i + k, i) for i in range(count - k)]
                lo_got = unpack(lax.ppermute(pack(lo_send), axis, up), lo_send)
                hi_got = unpack(lax.ppermute(pack(hi_send), axis, down), hi_send)
            lows.append(lo_got[0])
            highs.append(hi_got[0])
            if len(lo_got) > 1:
                received[axis] = (lo_got[1], hi_got[1])
        packet = jnp.concatenate(lows[::-1] + [packet] + highs, axis=dim)
    return packet, received


def box_geometry(statics, starts, totals, width, block):
    nx, ny, nz = (b + 2 * width for b in block)
    flat = nx * ny

    def to_box(chans):
        c = chans.shape[0]
        return chans.transpose(0, 3, 1, 2).reshape(c, nz, flat)

    st = to_box(statics)
    coeffb, flagb = st[0], st[1]
    pos = [starts[d] - width + jnp.arange(n, dtype=jnp.int32) for d, n in enumerate((nx, ny, nz))]
    px = jnp.broadcast_to(pos[0][None, :, None], (nz, nx, ny)).reshape(nz, flat)
    py = jnp.broadcast_to(pos[1][None, None, :], (nz, nx, ny)).reshape(nz, flat)
    pz = jnp.broadcast_to(pos[2][:, None], (nz, flat))
    pvals = (px, py, pz)
    in_domain = (
        (px >= 0) & (px < totals[0]) & (py >= 0) & (py < totals[1]) & (pz >= 0) & (pz < totals[2])
    )
    g_lo = [jnp.where(pvals[d] > 0, 1.0, flagb) for d in range(3)]
    g_hi = [jnp.where(pvals[d] < totals[d] - 1, 1.0, flagb) for d in range(3)]
    inverse_diag = jnp.where(in_domain, 1.0 / (coeffb * 3.5 + 3.0 * COARSE_PENALTY), 0.0)
    moves = ((4, ny), (4, 1), (3, 1))

    def face_dim(v, d):
        ax, stp = moves[d]
        low = lax.slice_in_dim(v, 0, 1, axis=d)
        high = lax.slice_in_dim(v, 1, 2, axis=d)
        tau = COARSE_PENALTY
        low_term = tau * g_lo[d] * low - tau * shift(high, ax, -stp)
        high_term = tau * g_hi[d] * high - tau * shift(low, ax, stp)
        return jnp.concatenate([low_term, high_term], axis=d)

    def apply_coarse(v):
        blk = coeffb * (3.5 * v - jnp.flip(v, 0) - jnp.flip(v, 1) - jnp.flip(v, 2))
        faces = face_dim(v, 0) + face_dim(v, 1) + face_dim(v, 2)
        return blk + faces

    def solve(chans):
        box = to_box(chans).reshape(2, 2, 2, nz, flat)
        center = 0.5 * (CHEB_HIGH + CHEB_LOW)
        half_width = 0.5 * (CHEB_HIGH - CHEB_LOW)
        sigma_value = center / half_width
        rho_now = 1.0 / sigma_value
        remain = box
        update = inverse_diag * remain / center
        result = update
        for sweep_num in range(CHEB - 1):
            remain = remain - apply_coarse(update)
            rho_next = 1.0 / (2.0 * sigma_value - rho_now)
            update = rho_next * rho_now * update + 2.0 * rho_next / half_width * (inverse_diag * remain)
            result = result + update
            rho_now = rho_next
        result = result.reshape(8, nz, nx, ny)

        def take(ranges):
            (x0, x1), (y0, y1), (z0, z1) = ranges
            return result[:, z0:z1, x0:x1, y0:y1].transpose(2, 3, 1, 0)

        return take

    return solve


def _onehot_tables():
    idx = np.arange(DEG1**3)
    picks = [idx // (DEG1 * DEG1), (idx // DEG1) % DEG1, idx % DEG1]
    return np.stack([(p[:, None] == np.arange(DEG1)[None, :]) for p in picks]).astype(np.float32)


ONEHOT = _onehot_tables()


def face_select():
    n = lax.broadcasted_iota(jnp.int32, (DEG1**3, 6 * 128), 0)
    c = lax.broadcasted_iota(jnp.int32, (DEG1**3, 6 * 128), 1)
    face, spot = c // 128, c % 128
    dim, side = face // 2, face % 2
    n0, n1, n2 = n // (DEG1 * DEG1), (n // DEG1) % DEG1, n % DEG1
    along = jnp.where(dim == 0, n0, jnp.where(dim == 1, n1, n2))
    rest = jnp.where(dim == 0, n1 * DEG1 + n2, jnp.where(dim == 1, n0 * DEG1 + n2, n0 * DEG1 + n1))
    return ((along == side * (DEG1 - 1)) & (spot == rest)).astype(jnp.float32)


def build_tables(basis, eigenvalues):
    eigen_table = None
    for pick in ONEHOT:
        pick = jnp.asarray(pick)
        part = lax.dot_general(
            jnp.dot(pick, basis, precision=HIGHEST, preferred_element_type=jnp.float32),
            pick,
            (((1,), (1,)), ((), ())),
            precision=HIGHEST,
            preferred_element_type=jnp.float32,
        )
        eigen_table = part if eigen_table is None else eigen_table * part
    spectrum = (
        eigenvalues[:, None, None] + eigenvalues[None, :, None] + eigenvalues[None, None, :]
    ).reshape(-1)
    points = jnp.array(np.array(GLL_POINTS), jnp.float32)
    linear = jnp.stack([(1.0 - points) * 0.5, (1.0 + points) * 0.5])
    restrict_table = (
        linear.T[:, None, None, :, None, None]
        * linear.T[None, :, None, None, :, None]
        * linear.T[None, None, :, None, None, :]
    ).reshape(DEG1**3, 8)
    return (eigen_table, spectrum, restrict_table)


def boundary_coefs(flag_values, starts, totals, penalty):
    result_list = []
    for dimension in range(3):
        position = starts[dimension] + lax.broadcasted_iota(jnp.int32, flag_values.shape, dimension)
        lower_coef = penalty * jnp.where(position > 0, 1.0, flag_values)
        upper_coef = penalty * jnp.where(position < totals[dimension] - 1, 1.0, flag_values)
        result_list.append((lower_coef[..., None, None, None], upper_coef[..., None, None, None]))
    return result_list


def eigen_apply(flat, eigen_table, scale):
    inside = jnp.dot(flat, eigen_table, precision=HIGHEST, preferred_element_type=jnp.float32)
    return lax.dot_general(
        inside * scale, eigen_table, (((1,), (1,)), ((), ())), precision=HIGHEST,
        preferred_element_type=jnp.float32,
    )


def mm(a, b):
    return jnp.dot(a, b, precision=HIGHEST, preferred_element_type=jnp.float32)


def mm_t(a, b):
    return lax.dot_general(
        a, b, (((1,), (1,)), ((), ())), precision=HIGHEST, preferred_element_type=jnp.float32
    )


def body(rhs, coeff, flags, basis, eigenvalues):
    eigen_table, spectrum, restrict_table = build_tables(basis, eigenvalues)
    shape_three = rhs.shape[:3]
    node_count = rhs.shape[3]
    count = rhs.size // node_count
    axes = ("gx", "yz", "grp")
    flag_values = flags.astype(jnp.float32)
    starts = tuple(lax.axis_index(a) * shape_three[d] for d, a in enumerate(axes))
    totals = tuple(shape_three[d] * lax.axis_size(a) for d, a in enumerate(axes))
    fine_coefs = boundary_coefs(flag_values, starts, totals, PENALTY)
    coeff2 = coeff.reshape(count, 1)
    block_scale = coeff2 * spectrum[None, :]
    inverse_scale = 1.0 / block_scale
    select = face_select()
    restrict_faces = lax.dot_general(
        restrict_table, select, (((0,), (0,)), ((), ())), precision=HIGHEST,
        preferred_element_type=jnp.float32,
    )
    wide = CHEB
    narrow = CHEB - 1

    rhs2 = rhs.reshape(count, node_count)
    smoothed0 = eigen_apply(rhs2, eigen_table, inverse_scale)
    q0 = mm(rhs2, restrict_table)
    s_faces = mm(smoothed0, select).reshape(shape_three + (6, 128))

    def face_of(faces, d, side, lo, hi):
        return lax.slice_in_dim(faces[..., 2 * d + side, :], lo, hi, axis=d)

    bx, by, bz = shape_three
    extras = {
        "gx": (face_of(s_faces, 0, 1, bx - 1, bx), face_of(s_faces, 0, 0, 0, 1)),
        "yz": (face_of(s_faces, 1, 1, by - 1, by), face_of(s_faces, 1, 0, 0, 1)),
    }
    z_count = lax.axis_size("grp")
    z_top, z_bottom = face_of(s_faces, 2, 1, bz - 1, bz), face_of(s_faces, 2, 0, 0, 1)
    if z_count == 2:
        me = lax.axis_index("grp")
        got = lax.ppermute(jnp.where(me == 0, z_top, z_bottom), "grp", [(0, 1), (1, 0)])
        z_recv = (jnp.where(me == 1, got, jnp.zeros_like(got)), jnp.where(me == 0, got, jnp.zeros_like(got)))
    else:
        z_recv = (
            lax.ppermute(z_top, "grp", [(i, i + 1) for i in range(z_count - 1)]),
            lax.ppermute(z_bottom, "grp", [(i + 1, i) for i in range(z_count - 1)]),
        )

    packet0 = jnp.concatenate(
        [q0.T.reshape((8,) + shape_three), jnp.stack([coeff, flag_values])], axis=0
    )
    box0, received = halo_box(packet0, wide, extras)
    received["grp"] = z_recv
    statics = box0[8:10]
    take0 = box_geometry(statics, starts, totals, wide, shape_three)(box0[:8])
    own = [(wide, wide + b) for b in shape_three]
    c0_own = take0(own).reshape(count, 8)
    u1 = DAMPING * (smoothed0 + mm_t(c0_own, restrict_table))

    u_faces = mm(u1, select).reshape(shape_three + (6, 128))
    terms = []
    for d, axis in enumerate(axes):
        block = shape_three[d]
        below = list(own)
        below[d] = (wide - 1, wide)
        above = list(own)
        above[d] = (wide + block, wide + block + 1)
        planes = []
        for rng, side, got in ((below, 1, received[axis][0]), (above, 0, received[axis][1])):
            c = take0(rng)
            lifted = mm(c.reshape(-1, 8), restrict_faces).reshape(c.shape[:3] + (6, 128))
            planes.append(DAMPING * (got + lifted[..., 2 * d + side, :]))
        low = u_faces[..., 2 * d, :]
        high = u_faces[..., 2 * d + 1, :]
        lower = jnp.concatenate([planes[0], lax.slice_in_dim(high, 0, block - 1, axis=d)], axis=d)
        upper = jnp.concatenate([lax.slice_in_dim(low, 1, block, axis=d), planes[1]], axis=d)
        lower_coef, upper_coef = fine_coefs[d]
        lower_coef = lower_coef.reshape(shape_three + (1,))
        upper_coef = upper_coef.reshape(shape_three + (1,))
        terms.append(lower_coef * low - PENALTY * lower)
        terms.append(upper_coef * high - PENALTY * upper)
    terms = jnp.stack(terms, axis=3).reshape(count, 6 * 128)
    faces = mm_t(terms, select)
    residual = rhs2 - (eigen_apply(u1, eigen_table, block_scale) + faces)
    smoothed1 = eigen_apply(residual, eigen_table, inverse_scale)
    q1 = mm(residual, restrict_table)
    box1, _ = halo_box(q1.T.reshape((8,) + shape_three), narrow)
    cut = wide - narrow
    statics1 = statics[:, cut:-cut, cut:-cut, cut:-cut]
    take1 = box_geometry(statics1, starts, totals, narrow, shape_three)(box1)
    c1_own = take1([(narrow, narrow + b) for b in shape_three]).reshape(count, 8)
    u2 = u1 + DAMPING * (smoothed1 + mm_t(c1_own, restrict_table))
    return u2.reshape(rhs.shape)


def solution(mesh):
    in_specs = (P("gx", "yz", "grp", None), P("gx", "yz", "grp"), P("gx", "yz", "grp"), P(), P())
    out_specs = P("gx", "yz", "grp", None)
    return jax.shard_map(body, mesh=mesh, in_specs=in_specs, out_specs=out_specs, check_vma=False)
```

```python
import jax
import jax.numpy as jnp
import numpy as np
from jax import lax
from jax.sharding import PartitionSpec as P

DEG1 = 8
ITERS = 2
CHEB = 4


PENALTY = 2.0
COARSE_PENALTY = 1.0
DAMPING = 0.5
CHEB_LOW = 0.1
CHEB_HIGH = 2.0
GLL_POINTS = (
    -1.0,
    -0.8717401485096066,
    -0.5917001814331423,
    -0.2092992179024789,
    0.2092992179024789,
    0.5917001814331423,
    0.8717401485096066,
    1.0,
)
HIGHEST = lax.Precision.HIGHEST


def face_traces(field, points):
    lower_list, upper_list = ([], [])
    for dimension, axis in enumerate(("gx", "yz", "grp")):
        count = lax.axis_size(axis)
        block = field.shape[dimension]
        node_axis = 3 + dimension
        high = lax.slice_in_dim(field, points - 1, points, axis=node_axis)
        low = lax.slice_in_dim(field, 0, 1, axis=node_axis)
        top = lax.slice_in_dim(high, block - 1, block, axis=dimension)
        bottom = lax.slice_in_dim(low, 0, 1, axis=dimension)
        if count == 2:
            me = lax.axis_index(axis)
            got = lax.ppermute(jnp.where(me == 0, top, bottom), axis, [(0, 1), (1, 0)])
            zero = jnp.zeros_like(got)
            from_below = jnp.where(me == 1, got, zero)
            from_above = jnp.where(me == 0, got, zero)
        else:
            from_below = lax.ppermute(top, axis, [(i, i + 1) for i in range(count - 1)])
            from_above = lax.ppermute(bottom, axis, [(i + 1, i) for i in range(count - 1)])
        lower_list.append(
            jnp.concatenate([from_below, lax.slice_in_dim(high, 0, block - 1, axis=dimension)], axis=dimension)
        )
        upper_list.append(
            jnp.concatenate([lax.slice_in_dim(low, 1, block, axis=dimension), from_above], axis=dimension)
        )
    return (lower_list, upper_list)


def shift(v, axis, s):
    size = v.shape[axis]
    zshape = list(v.shape)
    zshape[axis] = abs(s)
    zeros = jnp.zeros(zshape, v.dtype)
    if s > 0:
        return jnp.concatenate([lax.slice_in_dim(v, s, size, axis=axis), zeros], axis=axis)
    return jnp.concatenate([zeros, lax.slice_in_dim(v, 0, size + s, axis=axis)], axis=axis)


def halo_box(packet, width):
    for dim, axis in ((1, "gx"), (2, "yz"), (3, "grp")):
        count = lax.axis_size(axis)
        block = packet.shape[dim]
        lo_piece = lax.slice_in_dim(packet, block - width, block, axis=dim)
        hi_piece = lax.slice_in_dim(packet, 0, width, axis=dim)
        if count == 2:
            me = lax.axis_index(axis)
            got = lax.ppermute(jnp.where(me == 0, lo_piece, hi_piece), axis, [(0, 1), (1, 0)])
            zero = jnp.zeros_like(got)
            from_below = jnp.where(me == 1, got, zero)
            from_above = jnp.where(me == 0, got, zero)
        else:
            from_below = lax.ppermute(lo_piece, axis, [(i, i + 1) for i in range(count - 1)])
            from_above = lax.ppermute(hi_piece, axis, [(i + 1, i) for i in range(count - 1)])
        packet = jnp.concatenate([from_below, packet, from_above], axis=dim)
    return packet


def box_solver(coeff, flag_values, starts, totals, width):
    bx, by, bz = coeff.shape
    nx, ny, nz = bx + 2 * width, by + 2 * width, bz + 2 * width
    flat = nx * ny
    state = {}

    def to_box(chans):
        c = chans.shape[0]
        return chans.transpose(0, 3, 1, 2).reshape(c, nz, flat)

    def setup(coeffb, flagb):
        pos = [starts[d] - width + jnp.arange(n, dtype=jnp.int32) for d, n in enumerate((nx, ny, nz))]
        px = jnp.broadcast_to(pos[0][None, :, None], (nz, nx, ny)).reshape(nz, flat)
        py = jnp.broadcast_to(pos[1][None, None, :], (nz, nx, ny)).reshape(nz, flat)
        pz = jnp.broadcast_to(pos[2][:, None], (nz, flat))
        pvals = (px, py, pz)
        in_domain = (
            (px >= 0) & (px < totals[0]) & (py >= 0) & (py < totals[1]) & (pz >= 0) & (pz < totals[2])
        )
        state["coeff"] = coeffb
        state["g_lo"] = [jnp.where(pvals[d] > 0, 1.0, flagb) for d in range(3)]
        state["g_hi"] = [jnp.where(pvals[d] < totals[d] - 1, 1.0, flagb) for d in range(3)]
        state["inverse_diag"] = jnp.where(
            in_domain, 1.0 / (coeffb * 3.5 + 3.0 * COARSE_PENALTY), 0.0
        )

    moves = ((4, ny), (4, 1), (3, 1))

    def face_dim(v, d):
        ax, st = moves[d]
        low = lax.slice_in_dim(v, 0, 1, axis=d)
        high = lax.slice_in_dim(v, 1, 2, axis=d)
        tau = COARSE_PENALTY
        low_term = tau * state["g_lo"][d] * low - tau * shift(high, ax, -st)
        high_term = tau * state["g_hi"][d] * high - tau * shift(low, ax, st)
        return jnp.concatenate([low_term, high_term], axis=d)

    def apply_coarse(v):
        block = state["coeff"] * (3.5 * v - jnp.flip(v, 0) - jnp.flip(v, 1) - jnp.flip(v, 2))
        faces = face_dim(v, 0) + face_dim(v, 1) + face_dim(v, 2)
        return block + faces

    def solve(coarse_rhs):
        chans = coarse_rhs.transpose(3, 0, 1, 2)
        first = not state
        if first:
            chans = jnp.concatenate([chans, jnp.stack([coeff, flag_values])], axis=0)
        box = to_box(halo_box(chans, width))
        if first:
            setup(box[8], box[9])
            box = box[:8]
        box = box.reshape(2, 2, 2, nz, flat)
        inverse_diag = state["inverse_diag"]
        center = 0.5 * (CHEB_HIGH + CHEB_LOW)
        half_width = 0.5 * (CHEB_HIGH - CHEB_LOW)
        sigma_value = center / half_width
        rho_now = 1.0 / sigma_value
        remain = box
        update = inverse_diag * remain / center
        result = update
        for sweep_num in range(CHEB - 1):
            remain = remain - apply_coarse(update)
            rho_next = 1.0 / (2.0 * sigma_value - rho_now)
            update = rho_next * rho_now * update + 2.0 * rho_next / half_width * (inverse_diag * remain)
            result = result + update
            rho_now = rho_next
        own = result.reshape(8, nz, nx, ny)[:, width : width + bz, width : width + bx, width : width + by]
        return own.transpose(2, 3, 1, 0)

    return solve

def _onehot_tables():
    idx = np.arange(DEG1**3)
    picks = [idx // (DEG1 * DEG1), (idx // DEG1) % DEG1, idx % DEG1]
    return np.stack([(p[:, None] == np.arange(DEG1)[None, :]) for p in picks]).astype(np.float32)


ONEHOT = _onehot_tables()


def _restrict_table():
    points = np.array(GLL_POINTS, np.float32)
    linear = np.stack([(1.0 - points) * 0.5, (1.0 + points) * 0.5]).astype(np.float32)
    return (
        linear.T[:, None, None, :, None, None]
        * linear.T[None, :, None, None, :, None]
        * linear.T[None, None, :, None, None, :]
    ).reshape(DEG1**3, 8)


RESTRICT = _restrict_table()


def face_select():
    n = lax.broadcasted_iota(jnp.int32, (DEG1**3, 6 * 128), 0)
    c = lax.broadcasted_iota(jnp.int32, (DEG1**3, 6 * 128), 1)
    face, spot = c // 128, c % 128
    dim, side = face // 2, face % 2
    n0, n1, n2 = n // (DEG1 * DEG1), (n // DEG1) % DEG1, n % DEG1
    along = jnp.where(dim == 0, n0, jnp.where(dim == 1, n1, n2))
    rest = jnp.where(dim == 0, n1 * DEG1 + n2, jnp.where(dim == 1, n0 * DEG1 + n2, n0 * DEG1 + n1))
    return ((along == side * (DEG1 - 1)) & (spot == rest)).astype(jnp.float32)


def fine_face_term(flat, shape_three, coefs):
    select = face_select()
    faces = jnp.dot(flat, select, precision=HIGHEST, preferred_element_type=jnp.float32)
    faces = faces.reshape(shape_three + (6, 128))
    terms = []
    for dimension, axis in enumerate(("gx", "yz", "grp")):
        count = lax.axis_size(axis)
        block = shape_three[dimension]
        low = faces[..., 2 * dimension, :]
        high = faces[..., 2 * dimension + 1, :]
        top = lax.slice_in_dim(high, block - 1, block, axis=dimension)
        bottom = lax.slice_in_dim(low, 0, 1, axis=dimension)
        if count == 2:
            me = lax.axis_index(axis)
            got = lax.ppermute(jnp.where(me == 0, top, bottom), axis, [(0, 1), (1, 0)])
            zero = jnp.zeros_like(got)
            from_below = jnp.where(me == 1, got, zero)
            from_above = jnp.where(me == 0, got, zero)
        else:
            from_below = lax.ppermute(top, axis, [(i, i + 1) for i in range(count - 1)])
            from_above = lax.ppermute(bottom, axis, [(i + 1, i) for i in range(count - 1)])
        lower = jnp.concatenate([from_below, lax.slice_in_dim(high, 0, block - 1, axis=dimension)], axis=dimension)
        upper = jnp.concatenate([lax.slice_in_dim(low, 1, block, axis=dimension), from_above], axis=dimension)
        lower_coef, upper_coef = coefs[dimension]
        lower_coef = lower_coef.reshape(shape_three + (1,))
        upper_coef = upper_coef.reshape(shape_three + (1,))
        terms.append(lower_coef * low - PENALTY * lower)
        terms.append(upper_coef * high - PENALTY * upper)
    terms = jnp.stack(terms, axis=3).reshape(-1, 6 * 128)
    return lax.dot_general(
        terms, select, (((1,), (1,)), ((), ())), precision=HIGHEST, preferred_element_type=jnp.float32
    )


def build_tables(basis, eigenvalues):
    eigen_table = None
    for pick in ONEHOT:
        pick = jnp.asarray(pick)
        part = lax.dot_general(
            jnp.dot(pick, basis, precision=HIGHEST, preferred_element_type=jnp.float32),
            pick,
            (((1,), (1,)), ((), ())),
            precision=HIGHEST,
            preferred_element_type=jnp.float32,
        )
        eigen_table = part if eigen_table is None else eigen_table * part
    spectrum = (
        eigenvalues[:, None, None] + eigenvalues[None, :, None] + eigenvalues[None, None, :]
    ).reshape(-1)
    restrict_table = jnp.asarray(RESTRICT)
    return (eigen_table, spectrum, restrict_table)


def eigen_apply(values, eigen_table, scale):
    flat = values.reshape(-1, eigen_table.shape[0])
    inside = jnp.dot(flat, eigen_table, precision=HIGHEST, preferred_element_type=jnp.float32)
    scaled = inside * scale.reshape(flat.shape)
    back = lax.dot_general(
        scaled,
        eigen_table,
        (((1,), (1,)), ((), ())),
        precision=HIGHEST,
        preferred_element_type=jnp.float32,
    )
    return back.reshape(values.shape)


def boundary_coefs(flag_values, starts, totals, penalty):
    result_list = []
    for dimension in range(3):
        position = starts[dimension] + lax.broadcasted_iota(jnp.int32, flag_values.shape, dimension)
        lower_coef = penalty * jnp.where(position > 0, 1.0, flag_values)
        upper_coef = penalty * jnp.where(position < totals[dimension] - 1, 1.0, flag_values)
        result_list.append((lower_coef[..., None, None, None], upper_coef[..., None, None, None]))
    return result_list


def face_term(field, lower_list, upper_list, coefs, penalty):
    summed = jnp.zeros_like(field)
    points = field.shape[3]
    for dimension in range(3):
        node_axis = 3 + dimension
        low_face = lax.slice_in_dim(field, 0, 1, axis=node_axis)
        high_face = lax.slice_in_dim(field, points - 1, points, axis=node_axis)
        lower_coef, upper_coef = coefs[dimension]
        low_term = lower_coef * low_face - penalty * lower_list[dimension]
        high_term = upper_coef * high_face - penalty * upper_list[dimension]
        low_pad = [(0, 0)] * 6
        low_pad[node_axis] = (0, points - 1)
        high_pad = [(0, 0)] * 6
        high_pad[node_axis] = (points - 1, 0)
        summed = summed + jnp.pad(low_term, low_pad) + jnp.pad(high_term, high_pad)
    return summed


def coarse_block(corners, coarse_coeff):
    weight = coarse_coeff[..., None, None, None]
    return weight * (
        3.5 * corners - jnp.flip(corners, 3) - jnp.flip(corners, 4) - jnp.flip(corners, 5)
    )


def chebyshev(coarse_rhs, coarse_coeff, apply_coarse):
    center = 0.5 * (CHEB_HIGH + CHEB_LOW)
    half_width = 0.5 * (CHEB_HIGH - CHEB_LOW)
    sigma_value = center / half_width
    rho_now = 1.0 / sigma_value
    inverse_diag = (1.0 / (coarse_coeff * 3.5 + 3.0 * COARSE_PENALTY))[..., None]
    remain = coarse_rhs
    update = inverse_diag * remain / center
    result = update
    for sweep_num in range(CHEB - 1):
        remain = remain - apply_coarse(update)
        rho_next = 1.0 / (2.0 * sigma_value - rho_now)
        update = rho_next * rho_now * update + 2.0 * rho_next / half_width * (inverse_diag * remain)
        result = result + update
        rho_now = rho_next
    return result


def body(rhs, coeff, flags, basis, eigenvalues):
    eigen_table, spectrum, restrict_table = build_tables(basis, eigenvalues)
    shape_three = rhs.shape[:3]
    node_count = rhs.shape[3]
    flag_values = flags.astype(jnp.float32)
    starts = (
        lax.axis_index("gx") * shape_three[0],
        lax.axis_index("yz") * shape_three[1],
        lax.axis_index("grp") * shape_three[2],
    )
    totals = (
        shape_three[0] * lax.axis_size("gx"),
        shape_three[1] * lax.axis_size("yz"),
        shape_three[2] * lax.axis_size("grp"),
    )
    fine_coefs = boundary_coefs(flag_values, starts, totals, PENALTY)
    block_scale = coeff[..., None] * spectrum
    inverse_scale = 1.0 / block_scale

    def apply_fine(solution):
        faces = fine_face_term(solution.reshape(-1, node_count), shape_three, fine_coefs).reshape(
            solution.shape
        )
        return eigen_apply(solution, eigen_table, block_scale) + faces

    solve_coarse = box_solver(coeff, flag_values, starts, totals, CHEB - 1)
    solution = jnp.zeros_like(rhs)
    for iteration in range(ITERS):
        residual = rhs if iteration == 0 else rhs - apply_fine(solution)
        smoothed = eigen_apply(residual, eigen_table, inverse_scale)
        coarse_rhs = jnp.dot(
            residual.reshape(-1, node_count),
            restrict_table,
            precision=HIGHEST,
            preferred_element_type=jnp.float32,
        ).reshape(shape_three + (8,))
        coarse_sol = solve_coarse(coarse_rhs)
        lifted = lax.dot_general(
            coarse_sol.reshape(-1, 8),
            restrict_table,
            (((1,), (1,)), ((), ())),
            precision=HIGHEST,
            preferred_element_type=jnp.float32,
        ).reshape(rhs.shape)
        solution = solution + DAMPING * (smoothed + lifted)
    return solution


def solution(mesh):
    in_specs = (P("gx", "yz", "grp", None), P("gx", "yz", "grp"), P("gx", "yz", "grp"), P(), P())
    out_specs = P("gx", "yz", "grp", None)
    return jax.shard_map(body, mesh=mesh, in_specs=in_specs, out_specs=out_specs, check_vma=False)
```
